768 devices in a mesh: rep: 12 (over z_lo, core), row: 8 (over x, z_hi), col: 8 (over y).
Axes of the slice: x: 4, y: 8, z: 12 (z_hi: 2, z_lo: 6; z = z_hi * 6 + z_lo), core: 2. Of those that a mesh axis runs over, the one named last changes fastest.
Arguments:
- tokens: bfloat16 [1536, 4096], P('rep', 'row'), may hold values from -6 to 6
- gate_weight: bfloat16 [8, 1920, 4096], P('col', 'rep', 'row'), may hold values from -0.09375 to 0.09375
- up_weight: bfloat16 [8, 1920, 4096], P('col', 'rep', 'row'), may hold values from -0.09375 to 0.09375
- cotangent: bfloat16 [1536, 15360], P(('rep', 'row'), 'col'), may hold values from -5 to 5
Outputs:
- hidden: bfloat16 [1536, 15360], P(('rep', 'row'), 'col')
- grad_tokens: bfloat16 [1536, 4096], P(('rep', 'col'), 'row')
- grad_gate_weight: bfloat16 [8, 1920, 4096], P('col', 'rep', 'row')
- grad_up_weight: bfloat16 [8, 1920, 4096], P('col', 'rep', 'row')
The draws below stay inside these ranges and needn't reach their ends.
All inputs are finite; a program needn't handle non-finite values.
Results may differ from the reference program's by a relative error of at most 0.017.
Values may be sent and summed in bfloat16 or wider, within the bound.
No kernel may reach another device: no remote copies, remote signals or barrier semaphores. Data moves between devices by JAX's collectives and lax.ppermute only.
A program may use at most 32 MiB of HBM per device.

```python
import jax
import jax.numpy as jnp
from jax import lax

D = 4096
FF = 15360
TOK = 128
TOKENS = 1536
N_REP = 12
N_COL = 8


def raised(array, rng, source, target, blocks, factor):
    def block_of(axis_at):
        return (jnp.arange(array.shape[axis_at]) // (array.shape[axis_at] // blocks)).reshape((-1,) + (1,) * (array.ndim - 1 - axis_at))

    one_side = jax.random.permutation(rng, blocks)[block_of(target)]
    far = (block_of(target) + blocks // 2) % blocks
    return jnp.where((block_of(source) == one_side) | (block_of(source) == far), factor * array, array)


def block_levels(key, dims, cuts, low, largest):
    def one(dim, shards_of):
        draws = jax.random.uniform(jax.random.fold_in(jax.random.fold_in(key, 6), dim), (shards_of,), jnp.float32, low / len(cuts), largest / len(cuts))
        return jnp.repeat(jnp.exp(draws), dims[dim] // shards_of).reshape((-1,) + (1,) * (len(dims) - dim - 1))

    loudness = one(*cuts[0])
    for cut in cuts[1:]:
        loudness = loudness * one(*cut)
    return loudness


def centred(own_key, dims, spread, most, split=(), dtype=jnp.bfloat16):
    array = jax.random.normal(own_key, dims, jnp.float32) * spread
    if len(split) > 0:
        array = block_levels(own_key, dims, split, -0.22, 0.18) * array
    return jnp.clip(array, min=-most, max=most).astype(dtype)


def heavy_noise(stream_key, extent, spread, reach, pieces, heavy, dtype=jnp.bfloat16):
    entries = spread * jax.random.normal(stream_key, extent, jnp.float32)
    if pieces:
        entries = entries * block_levels(stream_key, extent, pieces, -0.22, 0.18)
    return jnp.clip(raised(entries, jax.random.fold_in(stream_key, 3), *heavy), -reach, reach).astype(dtype)


def setup_inputs(seed: int = 0) -> dict:
    seeds = jax.random.split(jax.random.key(seed), 5)
    tokens = centred(seeds[0], (TOKENS, D), 1.0, 6.0, ((0, 12), (1, 8)))
    gate_weight = centred(seeds[1], (N_COL, FF // N_COL, D), D ** -0.5, 0.09375, ((0, 8), (1, 12), (2, 8)))
    up_weight = centred(seeds[2], (N_COL, FF // N_COL, D), D ** -0.5, 0.09375, ((0, 8), (1, 12), (2, 8)))
    cotangent = heavy_noise(seeds[3], (TOKENS, FF), 0.25, 5.0, ((0, 96), (1, 8)), (0, 1, 96, 4.75))
    return dict(tokens=tokens, gate_weight=gate_weight, up_weight=up_weight, cotangent=cotangent)


def reference(tokens, gate_weight, up_weight, cotangent):
    gate_full = gate_weight.reshape(FF, D)
    up_full = up_weight.reshape(FF, D)
    contract = (((1,), (1,)), ((), ()))
    gate_pre = lax.dot_general(tokens, gate_full, contract, preferred_element_type=jnp.float32)
    up_pre = lax.dot_general(tokens, up_full, contract, preferred_element_type=jnp.float32)
    sigmoid_val = jax.nn.sigmoid(gate_pre)
    gated = gate_pre * sigmoid_val
    hidden = (gated * up_pre).astype(jnp.bfloat16)
    upstream = cotangent.astype(jnp.float32)
    grad_gate_pre = (upstream * up_pre * sigmoid_val * (1.0 + gate_pre * (1.0 - sigmoid_val))).astype(jnp.bfloat16)
    grad_up_pre = (upstream * gated).astype(jnp.bfloat16)
    grad_tokens = jnp.dot(grad_gate_pre, gate_full, preferred_element_type=jnp.float32)
    grad_tokens = grad_tokens + jnp.dot(grad_up_pre, up_full, preferred_element_type=jnp.float32)
    grad_tokens = grad_tokens.astype(jnp.bfloat16)
    over_rows = (((0,), (0,)), ((), ()))

    def replica_step(carry, blocks):
        token_rows, grads_gate, grads_up = blocks
        term_gate = lax.dot_general(grads_gate, token_rows, over_rows, preferred_element_type=jnp.float32)
        term_up = lax.dot_general(grads_up, token_rows, over_rows, preferred_element_type=jnp.float32)
        rounded = lax.optimization_barrier((term_gate.astype(jnp.bfloat16), term_up.astype(jnp.bfloat16)))
        return (carry[0] + rounded[0].astype(jnp.float32), carry[1] + rounded[1].astype(jnp.float32)), None

    start_sums = (jnp.zeros((FF, D), jnp.float32), jnp.zeros((FF, D), jnp.float32))
    blocks = (tokens.reshape(N_REP, TOK, D), grad_gate_pre.reshape(N_REP, TOK, FF), grad_up_pre.reshape(N_REP, TOK, FF))
    (sum_gate, sum_up), _ = lax.scan(replica_step, start_sums, blocks)
    inverse = 1.0 / N_REP
    grad_gate_weight = (sum_gate * inverse).astype(jnp.bfloat16).reshape(N_COL, FF // N_COL, D)
    grad_up_weight = (sum_up * inverse).astype(jnp.bfloat16).reshape(N_COL, FF // N_COL, D)
    return (hidden, grad_tokens, grad_gate_weight, grad_up_weight)
```

```python
import jax
import jax.numpy as jnp
from jax import lax
from jax.sharding import Mesh
from jax.sharding import PartitionSpec as P

REP = ("zl", "core")
ROW = ("x", "zh")


def body(tokens, gate_weight, up_weight, cotangent):
    replicas = lax.axis_size(REP)
    pair = jnp.concatenate([gate_weight, up_weight], 0)
    weight_pair = lax.all_gather(pair, REP, axis=1, tiled=True)
    hidden_units = weight_pair.shape[1]
    weight_rows = weight_pair.reshape(2 * hidden_units, weight_pair.shape[2])
    partial = jnp.einsum("td,hd->th", tokens, weight_rows, preferred_element_type=jnp.float32)
    summed = lax.psum_scatter(partial, "x", scatter_dimension=0, tiled=True)
    summed = lax.psum_scatter(summed, "zh", scatter_dimension=0, tiled=True)
    gate_pre = summed[:, :hidden_units]
    up_pre = summed[:, hidden_units:]
    sigmoid_val = jax.nn.sigmoid(gate_pre)
    gated = gate_pre * sigmoid_val
    hidden = (gated * up_pre).astype(jnp.bfloat16)
    upstream = cotangent.astype(jnp.float32)
    grad_gate_pre = (
        upstream * up_pre * sigmoid_val * (1.0 + gate_pre * (1.0 - sigmoid_val))
    ).astype(jnp.bfloat16)
    grad_up_pre = (upstream * gated).astype(jnp.bfloat16)
    pair_grads = jnp.concatenate([grad_gate_pre, grad_up_pre], 1)
    gathered = lax.all_gather(pair_grads, "zh", axis=0, tiled=True)
    gathered = lax.all_gather(gathered, "x", axis=0, tiled=True)
    replica_terms = jnp.einsum("th,td->hd", gathered, tokens, preferred_element_type=jnp.float32)
    replica_terms = replica_terms.reshape(weight_pair.shape)
    reduced = lax.psum_scatter(
        replica_terms.astype(jnp.bfloat16), REP, scatter_dimension=1, tiled=True
    ).astype(jnp.float32)
    grad_tokens = lax.psum_scatter(
        jnp.einsum("th,hd->td", gathered, weight_rows, preferred_element_type=jnp.float32),
        "col",
        scatter_dimension=0,
        tiled=True,
    )
    inverse = 1.0 / replicas
    averaged = reduced * inverse
    grad_gate_weight = averaged[0:1].astype(jnp.bfloat16)
    grad_up_weight = averaged[1:2].astype(jnp.bfloat16)
    return (hidden, grad_tokens.astype(jnp.bfloat16), grad_gate_weight, grad_up_weight)


def solution(mesh):
    n_rep, n_row, n_col = (mesh.shape[a] for a in ("rep", "row", "col"))
    devices = mesh.devices.reshape(n_rep // 2, 2, n_row // 2, 2, n_col)
    fine = Mesh(devices, ("zl", "core", "x", "zh", "col"))
    in_specs = (
        P(REP, ROW),
        P("col", REP, ROW),
        P("col", REP, ROW),
        P(REP + ROW, "col"),
    )
    out_specs = (
        P(REP + ROW, "col"),
        P(REP + ("col",), ROW),
        P("col", REP, ROW),
        P("col", REP, ROW),
    )
    return jax.shard_map(body, mesh=fine, in_specs=in_specs, out_specs=out_specs, check_vma=False)
```

```python
import jax
import jax.numpy as jnp
from jax import lax
from jax.sharding import Mesh
from jax.sharding import PartitionSpec as P

REP = ("zl", "core")
ROW = ("x", "zh")


def body(tokens, gate_weight, up_weight, cotangent):
    replicas = lax.axis_size(REP)
    pair = jnp.concatenate([gate_weight, up_weight], 0)
    shard_units = pair.shape[1]
    weight_pair = lax.all_gather(pair, REP, axis=1, tiled=True)
    copies = jnp.broadcast_to(tokens[None], (replicas,) + tokens.shape)
    all_tokens = lax.all_to_all(copies, REP, 0, 0, tiled=True)
    hidden_units = weight_pair.shape[1]
    weight_rows = weight_pair.reshape(2 * hidden_units, weight_pair.shape[2])
    partial = jnp.einsum("td,hd->th", tokens, weight_rows, preferred_element_type=jnp.float32)
    summed = lax.psum_scatter(partial, "x", scatter_dimension=0, tiled=True)
    summed = lax.psum_scatter(
        summed.astype(jnp.bfloat16), "zh", scatter_dimension=0, tiled=True
    ).astype(jnp.float32)
    gate_pre = summed[:, :hidden_units]
    up_pre = summed[:, hidden_units:]
    sigmoid_val = jax.nn.sigmoid(gate_pre)
    gated = gate_pre * sigmoid_val
    hidden = (gated * up_pre).astype(jnp.bfloat16)
    upstream = cotangent.astype(jnp.float32)
    grad_gate_pre = (
        upstream * up_pre * sigmoid_val * (1.0 + gate_pre * (1.0 - sigmoid_val))
    ).astype(jnp.bfloat16)
    grad_up_pre = (upstream * gated).astype(jnp.bfloat16)
    pair_grads = jnp.concatenate([grad_gate_pre, grad_up_pre], 1)
    gathered = lax.all_gather(pair_grads, "zh", axis=0, tiled=True)
    gathered = lax.all_gather(gathered, "x", axis=0, tiled=True)
    grad_tokens = lax.psum_scatter(
        jnp.einsum("th,hd->td", gathered, weight_rows, preferred_element_type=jnp.float32),
        "col",
        scatter_dimension=0,
        tiled=True,
    )
    rows = gathered.shape[0]
    by_owner = gathered.reshape(rows, 2, replicas, shard_units).transpose(2, 0, 1, 3)
    owned = lax.all_to_all(by_owner, REP, 0, 0, tiled=True)
    terms = jnp.einsum("qtkh,qtd->qkhd", owned, all_tokens, preferred_element_type=jnp.float32)
    rounded = lax.reduce_precision(terms, exponent_bits=8, mantissa_bits=7)
    averaged = jnp.sum(rounded, axis=0) * (1.0 / replicas)
    grad_gate_weight = averaged[0:1].astype(jnp.bfloat16)
    grad_up_weight = averaged[1:2].astype(jnp.bfloat16)
    return (hidden, grad_tokens.astype(jnp.bfloat16), grad_gate_weight, grad_up_weight)


def solution(mesh):
    n_rep, n_row, n_col = (mesh.shape[a] for a in ("rep", "row", "col"))
    devices = mesh.devices.reshape(n_rep // 2, 2, n_row // 2, 2, n_col)
    fine = Mesh(devices, ("zl", "core", "x", "zh", "col"))
    in_specs = (
        P(REP, ROW),
        P("col", REP, ROW),
        P("col", REP, ROW),
        P(REP + ROW, "col"),
    )
    out_specs = (
        P(REP + ROW, "col"),
        P(REP + ("col",), ROW),
        P("col", REP, ROW),
        P("col", REP, ROW),
    )
    return jax.shard_map(body, mesh=fine, in_specs=in_specs, out_specs=out_specs, check_vma=False)
```

```python
import jax
import jax.numpy as jnp
from jax import lax
from jax.sharding import Mesh
from jax.sharding import PartitionSpec as P

REP = ("zl", "core")
ROW = ("x", "zh")


def body(tokens, gate_weight, up_weight, cotangent):
    replicas = lax.axis_size(REP)
    shard_units = gate_weight.shape[1]
    gate_whole = lax.all_gather(gate_weight, REP, axis=1, tiled=True)
    up_copies = jnp.broadcast_to(up_weight, (replicas,) + up_weight.shape[1:])
    up_whole = lax.all_to_all(up_copies, REP, 0, 0, tiled=True)
    weight_pair = jnp.concatenate([gate_whole, up_whole.reshape(gate_whole.shape)], 0)
    copies = jnp.broadcast_to(tokens[None], (replicas,) + tokens.shape)
    all_tokens = lax.all_to_all(copies, REP, 0, 0, tiled=True)
    hidden_units = weight_pair.shape[1]
    weight_rows = weight_pair.reshape(2 * hidden_units, weight_pair.shape[2])
    partial = jnp.einsum("td,hd->th", tokens, weight_rows, preferred_element_type=jnp.float32)
    summed = lax.psum_scatter(partial, "x", scatter_dimension=0, tiled=True)
    summed = lax.psum_scatter(
        summed.astype(jnp.bfloat16), "zh", scatter_dimension=0, tiled=True
    ).astype(jnp.float32)
    gate_pre = summed[:, :hidden_units]
    up_pre = summed[:, hidden_units:]
    sigmoid_val = jax.nn.sigmoid(gate_pre)
    gated = gate_pre * sigmoid_val
    hidden = (gated * up_pre).astype(jnp.bfloat16)
    upstream = cotangent.astype(jnp.float32)
    grad_gate_pre = (
        upstream * up_pre * sigmoid_val * (1.0 + gate_pre * (1.0 - sigmoid_val))
    ).astype(jnp.bfloat16)
    grad_up_pre = (upstream * gated).astype(jnp.bfloat16)
    pair_grads = jnp.concatenate([grad_gate_pre, grad_up_pre], 1)
    gathered = lax.all_gather(pair_grads, "zh", axis=0, tiled=True)
    gathered = lax.all_gather(gathered, "x", axis=0, tiled=True)
    n_col = lax.axis_size("col")
    token_partial = jnp.einsum("th,hd->td", gathered, weight_rows, preferred_element_type=jnp.float32)
    token_chunks = token_partial.reshape(n_col, token_partial.shape[0] // n_col, token_partial.shape[1])
    grad_tokens = jnp.sum(lax.all_to_all(token_chunks, "col", 0, 0, tiled=True), axis=0)
    rows = gathered.shape[0]
    by_owner = gathered.reshape(rows, 2, replicas, shard_units).transpose(2, 0, 1, 3)
    owned = lax.all_to_all(by_owner, REP, 0, 0, tiled=True)
    terms = jnp.einsum("qtkh,qtd->qkhd", owned, all_tokens, preferred_element_type=jnp.float32)
    rounded = lax.reduce_precision(terms, exponent_bits=8, mantissa_bits=7)
    averaged = jnp.sum(rounded, axis=0) * (1.0 / replicas)
    grad_gate_weight = averaged[0:1].astype(jnp.bfloat16)
    grad_up_weight = averaged[1:2].astype(jnp.bfloat16)
    return (hidden, grad_tokens.astype(jnp.bfloat16), grad_gate_weight, grad_up_weight)


def solution(mesh):
    n_rep, n_row, n_col = (mesh.shape[a] for a in ("rep", "row", "col"))
    devices = mesh.devices.reshape(n_rep // 2, 2, n_row // 2, 2, n_col)
    fine = Mesh(devices, ("zl", "core", "x", "zh", "col"))
    in_specs = (
        P(REP, ROW),
        P("col", REP, ROW),
        P("col", REP, ROW),
        P(REP + ROW, "col"),
    )
    out_specs = (
        P(REP + ROW, "col"),
        P(REP + ("col",), ROW),
        P("col", REP, ROW),
        P("col", REP, ROW),
    )
    return jax.shard_map(body, mesh=fine, in_specs=in_specs, out_specs=out_specs, check_vma=False)
```

```python
import jax
import jax.numpy as jnp
from jax import lax
from jax.sharding import Mesh
from jax.sharding import PartitionSpec as P

REP = ("zl", "core")
ROW = ("x", "zh")


def body(tokens, gate_weight, up_weight, cotangent):
    replicas = lax.axis_size(REP)
    pair = jnp.concatenate([gate_weight, up_weight], 0)
    shard_units = pair.shape[1]
    weight_pair = lax.all_gather(pair, REP, axis=1, tiled=True)
    copies = jnp.broadcast_to(tokens[None], (replicas,) + tokens.shape)
    all_tokens = lax.all_to_all(copies, REP, 0, 0, tiled=True)
    hidden_units = weight_pair.shape[1]
    weight_rows = weight_pair.reshape(2 * hidden_units, weight_pair.shape[2])
    partial = jnp.einsum("td,hd->th", tokens, weight_rows, preferred_element_type=jnp.float32)
    summed = lax.psum_scatter(partial, ROW, scatter_dimension=0, tiled=True)
    gate_pre = summed[:, :hidden_units]
    up_pre = summed[:, hidden_units:]
    sigmoid_val = jax.nn.sigmoid(gate_pre)
    gated = gate_pre * sigmoid_val
    hidden = (gated * up_pre).astype(jnp.bfloat16)
    upstream = cotangent.astype(jnp.float32)
    grad_gate_pre = (
        upstream * up_pre * sigmoid_val * (1.0 + gate_pre * (1.0 - sigmoid_val))
    ).astype(jnp.bfloat16)
    grad_up_pre = (upstream * gated).astype(jnp.bfloat16)
    pair_grads = jnp.concatenate([grad_gate_pre, grad_up_pre], 1)
    gathered = lax.all_gather(pair_grads, ROW, axis=0, tiled=True)
    grad_tokens = lax.psum_scatter(
        jnp.einsum("th,hd->td", gathered, weight_rows, preferred_element_type=jnp.float32),
        "col",
        scatter_dimension=0,
        tiled=True,
    )
    rows = gathered.shape[0]
    by_owner = gathered.reshape(rows, 2, replicas, shard_units).transpose(2, 0, 1, 3)
    owned = lax.all_to_all(by_owner, REP, 0, 0, tiled=True)
    terms = jnp.einsum("qtkh,qtd->qkhd", owned, all_tokens, preferred_element_type=jnp.float32)
    rounded = lax.reduce_precision(terms, exponent_bits=8, mantissa_bits=7)
    averaged = jnp.sum(rounded, axis=0) * (1.0 / replicas)
    grad_gate_weight = averaged[0:1].astype(jnp.bfloat16)
    grad_up_weight = averaged[1:2].astype(jnp.bfloat16)
    return (hidden, grad_tokens.astype(jnp.bfloat16), grad_gate_weight, grad_up_weight)


def solution(mesh):
    n_rep, n_row, n_col = (mesh.shape[a] for a in ("rep", "row", "col"))
    devices = mesh.devices.reshape(n_rep // 2, 2, n_row // 2, 2, n_col)
    fine = Mesh(devices, ("zl", "core", "x", "zh", "col"))
    in_specs = (
        P(REP, ROW),
        P("col", REP, ROW),
        P("col", REP, ROW),
        P(REP + ROW, "col"),
    )
    out_specs = (
        P(REP + ROW, "col"),
        P(REP + ("col",), ROW),
        P("col", REP, ROW),
        P("col", REP, ROW),
    )
    return jax.shard_map(body, mesh=fine, in_specs=in_specs, out_specs=out_specs, check_vma=False)
```

```python
import jax
import jax.numpy as jnp
from jax import lax
from jax.sharding import Mesh
from jax.sharding import PartitionSpec as P

REP = ("zl", "core")
ROW = ("x", "zh")


def body(tokens, gate_weight, up_weight, cotangent):
    replicas = lax.axis_size(REP)
    pair = jnp.concatenate([gate_weight, up_weight], 0)
    shard_units = pair.shape[1]
    weight_pair = lax.all_gather(pair, REP, axis=1, tiled=True)
    copies = jnp.broadcast_to(tokens[None], (replicas,) + tokens.shape)
    all_tokens = lax.all_to_all(copies, REP, 0, 0, tiled=True)
    hidden_units = weight_pair.shape[1]
    weight_rows = weight_pair.reshape(2 * hidden_units, weight_pair.shape[2])
    partial = jnp.einsum("td,hd->th", tokens, weight_rows, preferred_element_type=jnp.float32)
    swap = [(0, 1), (1, 0)]
    upper = lax.axis_index("zh")
    partner_cot = lax.ppermute(cotangent, "zh", swap)
    summed = lax.psum_scatter(partial, "x", scatter_dimension=0, tiled=True)
    summed = summed + lax.ppermute(summed.astype(jnp.bfloat16), "zh", swap).astype(jnp.float32)
    gate_pre = summed[:, :hidden_units]
    up_pre = summed[:, hidden_units:]
    sigmoid_val = jax.nn.sigmoid(gate_pre)
    gated = gate_pre * sigmoid_val
    hidden = (gated * up_pre).astype(jnp.bfloat16)
    pair_cot = jnp.where(
        upper == 0,
        jnp.concatenate([cotangent, partner_cot], 0),
        jnp.concatenate([partner_cot, cotangent], 0),
    )
    upstream = pair_cot.astype(jnp.float32)
    grad_gate_pre = (
        upstream * up_pre * sigmoid_val * (1.0 + gate_pre * (1.0 - sigmoid_val))
    ).astype(jnp.bfloat16)
    grad_up_pre = (upstream * gated).astype(jnp.bfloat16)
    pair_grads = jnp.concatenate([grad_gate_pre, grad_up_pre], 1)
    gathered = lax.all_gather(pair_grads, "x", axis=0, tiled=True)
    own_rows = cotangent.shape[0]
    hidden = lax.dynamic_slice_in_dim(hidden, upper * own_rows, own_rows, 0)
    grad_tokens = lax.psum_scatter(
        jnp.einsum("th,hd->td", gathered, weight_rows, preferred_element_type=jnp.float32),
        "col",
        scatter_dimension=0,
        tiled=True,
    )
    rows = gathered.shape[0]
    by_owner = gathered.reshape(rows, 2, replicas, shard_units).transpose(2, 0, 1, 3)
    owned = lax.all_to_all(by_owner, REP, 0, 0, tiled=True)
    terms = jnp.einsum("qtkh,qtd->qkhd", owned, all_tokens, preferred_element_type=jnp.float32)
    rounded = lax.reduce_precision(terms, exponent_bits=8, mantissa_bits=7)
    averaged = jnp.sum(rounded, axis=0) * (1.0 / replicas)
    grad_gate_weight = averaged[0:1].astype(jnp.bfloat16)
    grad_up_weight = averaged[1:2].astype(jnp.bfloat16)
    return (hidden, grad_tokens.astype(jnp.bfloat16), grad_gate_weight, grad_up_weight)


def solution(mesh):
    n_rep, n_row, n_col = (mesh.shape[a] for a in ("rep", "row", "col"))
    devices = mesh.devices.reshape(n_rep // 2, 2, n_row // 2, 2, n_col)
    fine = Mesh(devices, ("zl", "core", "x", "zh", "col"))
    in_specs = (
        P(REP, ROW),
        P("col", REP, ROW),
        P("col", REP, ROW),
        P(REP + ROW, "col"),
    )
    out_specs = (
        P(REP + ROW, "col"),
        P(REP + ("col",), ROW),
        P("col", REP, ROW),
        P("col", REP, ROW),
    )
    return jax.shard_map(body, mesh=fine, in_specs=in_specs, out_specs=out_specs, check_vma=False)
```

```python
import jax
import jax.numpy as jnp
from jax import lax
from jax.sharding import Mesh
from jax.sharding import PartitionSpec as P

REP = ("zl", "core")
ROW = ("x", "zh")


def ring_reduce_scatter(values, axis):
    n = lax.axis_size(axis)
    i = lax.axis_index(axis)
    blocks = values.reshape(n, values.shape[0] // n, values.shape[1])
    half = values.shape[1] // 2
    forward = [(j, (j + 1) % n) for j in range(n)]
    backward = [(j, (j - 1) % n) for j in range(n)]

    def own(block, lo):
        return lax.dynamic_index_in_dim(blocks, block % n, 0, keepdims=False)[:, lo:lo + half]

    right = own(i + n - 1, 0)
    left = own(i + 1, half)
    for step in range(n - 1):
        right = lax.ppermute(right, axis, forward) + own(i + 2 * n - 2 - step, 0)
        left = lax.ppermute(left, axis, backward) + own(i + 2 + step, half)
    return jnp.concatenate([right, left], 1)


def body(tokens, gate_weight, up_weight, cotangent):
    replicas = lax.axis_size(REP)
    pair = jnp.concatenate([gate_weight, up_weight], 0)
    shard_units = pair.shape[1]
    weight_pair = lax.all_gather(pair, REP, axis=1, tiled=True)
    copies = jnp.broadcast_to(tokens[None], (replicas,) + tokens.shape)
    all_tokens = lax.all_to_all(copies, REP, 0, 0, tiled=True)
    hidden_units = weight_pair.shape[1]
    weight_rows = weight_pair.reshape(2 * hidden_units, weight_pair.shape[2])
    partial = jnp.einsum("td,hd->th", tokens, weight_rows, preferred_element_type=jnp.float32)
    swap = [(0, 1), (1, 0)]
    upper = lax.axis_index("zh")
    partner_cot = lax.ppermute(cotangent, "zh", swap)
    summed = ring_reduce_scatter(partial, "x")
    summed = summed + lax.ppermute(summed.astype(jnp.bfloat16), "zh", swap).astype(jnp.float32)
    gate_pre = summed[:, :hidden_units]
    up_pre = summed[:, hidden_units:]
    sigmoid_val = jax.nn.sigmoid(gate_pre)
    gated = gate_pre * sigmoid_val
    hidden = (gated * up_pre).astype(jnp.bfloat16)
    pair_cot = jnp.where(
        upper == 0,
        jnp.concatenate([cotangent, partner_cot], 0),
        jnp.concatenate([partner_cot, cotangent], 0),
    )
    upstream = pair_cot.astype(jnp.float32)
    grad_gate_pre = (
        upstream * up_pre * sigmoid_val * (1.0 + gate_pre * (1.0 - sigmoid_val))
    ).astype(jnp.bfloat16)
    grad_up_pre = (upstream * gated).astype(jnp.bfloat16)
    pair_grads = jnp.concatenate([grad_gate_pre, grad_up_pre], 1)
    gathered = lax.all_gather(pair_grads, "x", axis=0, tiled=True)
    own_rows = cotangent.shape[0]
    hidden = lax.dynamic_slice_in_dim(hidden, upper * own_rows, own_rows, 0)
    grad_tokens = lax.psum_scatter(
        jnp.einsum("th,hd->td", gathered, weight_rows, preferred_element_type=jnp.float32),
        "col",
        scatter_dimension=0,
        tiled=True,
    )
    rows = gathered.shape[0]
    by_owner = gathered.reshape(rows, 2, replicas, shard_units).transpose(2, 0, 1, 3)
    owned = lax.all_to_all(by_owner, REP, 0, 0, tiled=True)
    terms = jnp.einsum("qtkh,qtd->qkhd", owned, all_tokens, preferred_element_type=jnp.float32)
    rounded = lax.reduce_precision(terms, exponent_bits=8, mantissa_bits=7)
    averaged = jnp.sum(rounded, axis=0) * (1.0 / replicas)
    grad_gate_weight = averaged[0:1].astype(jnp.bfloat16)
    grad_up_weight = averaged[1:2].astype(jnp.bfloat16)
    return (hidden, grad_tokens.astype(jnp.bfloat16), grad_gate_weight, grad_up_weight)


def solution(mesh):
    n_rep, n_row, n_col = (mesh.shape[a] for a in ("rep", "row", "col"))
    devices = mesh.devices.reshape(n_rep // 2, 2, n_row // 2, 2, n_col)
    fine = Mesh(devices, ("zl", "core", "x", "zh", "col"))
    in_specs = (
        P(REP, ROW),
        P("col", REP, ROW),
        P("col", REP, ROW),
        P(REP + ROW, "col"),
    )
    out_specs = (
        P(REP + ROW, "col"),
        P(REP + ("col",), ROW),
        P("col", REP, ROW),
        P("col", REP, ROW),
    )
    return jax.shard_map(body, mesh=fine, in_specs=in_specs, out_specs=out_specs, check_vma=False)
```

```python
import jax
import jax.numpy as jnp
from jax import lax
from jax.sharding import Mesh
from jax.sharding import PartitionSpec as P

REP = ("zl", "core")
ROW = ("x", "zh")


def body(tokens, gate_weight, up_weight, cotangent):
    replicas = lax.axis_size(REP)
    pair = jnp.concatenate([gate_weight, up_weight], 0)
    shard_units = pair.shape[1]
    stacked = lax.all_gather(pair, REP, axis=0, tiled=False)
    copies = jnp.broadcast_to(tokens[None], (replicas,) + tokens.shape)
    all_tokens = lax.all_to_all(copies, REP, 0, 0, tiled=True)
    hidden_units = replicas * shard_units
    partial = jnp.einsum("td,rkjd->tkrj", tokens, stacked, preferred_element_type=jnp.float32)
    partial = partial.reshape(tokens.shape[0], 2 * hidden_units)
    swap = [(0, 1), (1, 0)]
    upper = lax.axis_index("zh")
    partner_cot = lax.ppermute(cotangent, "zh", swap)
    summed = lax.psum_scatter(partial, "x", scatter_dimension=0, tiled=True)
    summed = summed + lax.ppermute(summed.astype(jnp.bfloat16), "zh", swap).astype(jnp.float32)
    gate_pre = summed[:, :hidden_units]
    up_pre = summed[:, hidden_units:]
    sigmoid_val = jax.nn.sigmoid(gate_pre)
    gated = gate_pre * sigmoid_val
    hidden = (gated * up_pre).astype(jnp.bfloat16)
    pair_cot = jnp.where(
        upper == 0,
        jnp.concatenate([cotangent, partner_cot], 0),
        jnp.concatenate([partner_cot, cotangent], 0),
    )
    upstream = pair_cot.astype(jnp.float32)
    grad_gate_pre = (
        upstream * up_pre * sigmoid_val * (1.0 + gate_pre * (1.0 - sigmoid_val))
    ).astype(jnp.bfloat16)
    grad_up_pre = (upstream * gated).astype(jnp.bfloat16)
    pair_grads = jnp.concatenate([grad_gate_pre, grad_up_pre], 1)
    gathered = lax.all_gather(pair_grads, "x", axis=0, tiled=True)
    own_rows = cotangent.shape[0]
    hidden = lax.dynamic_slice_in_dim(hidden, upper * own_rows, own_rows, 0)
    grad_tokens = lax.psum_scatter(
        jnp.einsum(
            "tkrj,rkjd->td",
            gathered.reshape(gathered.shape[0], 2, replicas, shard_units),
            stacked,
            preferred_element_type=jnp.float32,
        ),
        "col",
        scatter_dimension=0,
        tiled=True,
    )
    rows = gathered.shape[0]
    by_owner = gathered.reshape(rows, 2, replicas, shard_units).transpose(2, 0, 1, 3)
    owned = lax.all_to_all(by_owner, REP, 0, 0, tiled=True)
    terms = jnp.einsum("qtkh,qtd->qkhd", owned, all_tokens, preferred_element_type=jnp.float32)
    rounded = lax.reduce_precision(terms, exponent_bits=8, mantissa_bits=7)
    averaged = jnp.sum(rounded, axis=0) * (1.0 / replicas)
    grad_gate_weight = averaged[0:1].astype(jnp.bfloat16)
    grad_up_weight = averaged[1:2].astype(jnp.bfloat16)
    return (hidden, grad_tokens.astype(jnp.bfloat16), grad_gate_weight, grad_up_weight)


def solution(mesh):
    n_rep, n_row, n_col = (mesh.shape[a] for a in ("rep", "row", "col"))
    devices = mesh.devices.reshape(n_rep // 2, 2, n_row // 2, 2, n_col)
    fine = Mesh(devices, ("zl", "core", "x", "zh", "col"))
    in_specs = (
        P(REP, ROW),
        P("col", REP, ROW),
        P("col", REP, ROW),
        P(REP + ROW, "col"),
    )
    out_specs = (
        P(REP + ROW, "col"),
        P(REP + ("col",), ROW),
        P("col", REP, ROW),
        P("col", REP, ROW),
    )
    return jax.shard_map(body, mesh=fine, in_specs=in_specs, out_specs=out_specs, check_vma=False)
```

```python
import jax
import jax.numpy as jnp
from jax import lax
from jax.sharding import Mesh
from jax.sharding import PartitionSpec as P

REP = ("zl", "core")
ROW = ("x", "zh")


def body(tokens, gate_weight, up_weight, cotangent):
    replicas = lax.axis_size(REP)
    pair = jnp.concatenate([gate_weight, up_weight], 0)
    shard_units = pair.shape[1]
    stacked = lax.all_gather(pair, REP, axis=0, tiled=False)
    copies = jnp.broadcast_to(tokens[None], (replicas,) + tokens.shape)
    all_tokens = lax.all_to_all(copies, REP, 0, 0, tiled=True)
    hidden_units = replicas * shard_units
    partial = jnp.einsum("td,rkjd->tkrj", tokens, stacked, preferred_element_type=jnp.float32)
    partial = partial.reshape(tokens.shape[0], 2 * hidden_units)
    swap = [(0, 1), (1, 0)]
    upper = lax.axis_index("zh")
    partner_cot = lax.ppermute(cotangent, "zh", swap)
    summed = lax.psum_scatter(partial, "x", scatter_dimension=0, tiled=True)
    summed = summed + lax.ppermute(summed.astype(jnp.bfloat16), "zh", swap).astype(jnp.float32)
    gate_pre = summed[:, :hidden_units]
    up_pre = summed[:, hidden_units:]
    sigmoid_val = jax.nn.sigmoid(gate_pre)
    gated = gate_pre * sigmoid_val
    hidden = (gated * up_pre).astype(jnp.bfloat16)
    pair_cot = jnp.where(
        upper == 0,
        jnp.concatenate([cotangent, partner_cot], 0),
        jnp.concatenate([partner_cot, cotangent], 0),
    )
    upstream = pair_cot.astype(jnp.float32)
    grad_gate_pre = (
        upstream * up_pre * sigmoid_val * (1.0 + gate_pre * (1.0 - sigmoid_val))
    ).astype(jnp.bfloat16)
    grad_up_pre = (upstream * gated).astype(jnp.bfloat16)
    pair_grads = jnp.concatenate([grad_gate_pre, grad_up_pre], 1)
    gathered = lax.all_gather(pair_grads, "x", axis=0, tiled=True)
    own_rows = cotangent.shape[0]
    hidden = lax.dynamic_slice_in_dim(hidden, upper * own_rows, own_rows, 0)
    token_partial = jnp.einsum(
        "tkrj,rkjd->td",
        gathered.reshape(gathered.shape[0], 2, replicas, shard_units),
        stacked,
        preferred_element_type=jnp.float32,
    )
    n_col = lax.axis_size("col")
    token_chunks = token_partial.reshape(n_col, token_partial.shape[0] // n_col, token_partial.shape[1])
    grad_tokens = jnp.sum(lax.all_to_all(token_chunks, "col", 0, 0, tiled=True), axis=0)
    rows = gathered.shape[0]
    by_owner = gathered.reshape(rows, 2, replicas, shard_units).transpose(2, 0, 1, 3)
    owned = lax.all_to_all(by_owner, REP, 0, 0, tiled=True)
    terms = jnp.einsum("qtkh,qtd->qkhd", owned, all_tokens, preferred_element_type=jnp.float32)
    rounded = lax.reduce_precision(terms, exponent_bits=8, mantissa_bits=7)
    averaged = jnp.sum(rounded, axis=0) * (1.0 / replicas)
    grad_gate_weight = averaged[0:1].astype(jnp.bfloat16)
    grad_up_weight = averaged[1:2].astype(jnp.bfloat16)
    return (hidden, grad_tokens.astype(jnp.bfloat16), grad_gate_weight, grad_up_weight)


def solution(mesh):
    n_rep, n_row, n_col = (mesh.shape[a] for a in ("rep", "row", "col"))
    devices = mesh.devices.reshape(n_rep // 2, 2, n_row // 2, 2, n_col)
    fine = Mesh(devices, ("zl", "core", "x", "zh", "col"))
    in_specs = (
        P(REP, ROW),
        P("col", REP, ROW),
        P("col", REP, ROW),
        P(REP + ROW, "col"),
    )
    out_specs = (
        P(REP + ROW, "col"),
        P(REP + ("col",), ROW),
        P("col", REP, ROW),
        P("col", REP, ROW),
    )
    return jax.shard_map(body, mesh=fine, in_specs=in_specs, out_specs=out_specs, check_vma=False)
```

```python
import jax
import jax.numpy as jnp
from jax import lax
from jax.sharding import Mesh
from jax.sharding import PartitionSpec as P

REP = ("zl", "core")
ROW = ("x", "zh")


def body(tokens, gate_weight, up_weight, cotangent):
    replicas = lax.axis_size(REP)
    pair = jnp.concatenate([gate_weight, up_weight], 0)
    shard_units = pair.shape[1]
    stacked = lax.all_gather(pair, "zl", axis=0, tiled=False)
    stacked = lax.all_gather(stacked, "core", axis=1, tiled=False)
    stacked = stacked.reshape((replicas,) + pair.shape)
    copies = jnp.broadcast_to(tokens[None], (replicas,) + tokens.shape)
    all_tokens = lax.all_to_all(copies, REP, 0, 0, tiled=True)
    hidden_units = replicas * shard_units
    partial = jnp.einsum("td,rkjd->tkrj", tokens, stacked, preferred_element_type=jnp.float32)
    partial = partial.reshape(tokens.shape[0], 2 * hidden_units)
    swap = [(0, 1), (1, 0)]
    upper = lax.axis_index("zh")
    partner_cot = lax.ppermute(cotangent, "zh", swap)
    summed = lax.psum_scatter(partial, "x", scatter_dimension=0, tiled=True)
    summed = summed + lax.ppermute(summed.astype(jnp.bfloat16), "zh", swap).astype(jnp.float32)
    gate_pre = summed[:, :hidden_units]
    up_pre = summed[:, hidden_units:]
    sigmoid_val = jax.nn.sigmoid(gate_pre)
    gated = gate_pre * sigmoid_val
    hidden = (gated * up_pre).astype(jnp.bfloat16)
    pair_cot = jnp.where(
        upper == 0,
        jnp.concatenate([cotangent, partner_cot], 0),
        jnp.concatenate([partner_cot, cotangent], 0),
    )
    upstream = pair_cot.astype(jnp.float32)
    grad_gate_pre = (
        upstream * up_pre * sigmoid_val * (1.0 + gate_pre * (1.0 - sigmoid_val))
    ).astype(jnp.bfloat16)
    grad_up_pre = (upstream * gated).astype(jnp.bfloat16)
    pair_grads = jnp.concatenate([grad_gate_pre, grad_up_pre], 1)
    gathered = lax.all_gather(pair_grads, "x", axis=0, tiled=True)
    own_rows = cotangent.shape[0]
    hidden = lax.dynamic_slice_in_dim(hidden, upper * own_rows, own_rows, 0)
    grad_tokens = lax.psum_scatter(
        jnp.einsum(
            "tkrj,rkjd->td",
            gathered.reshape(gathered.shape[0], 2, replicas, shard_units),
            stacked,
            preferred_element_type=jnp.float32,
        ),
        "col",
        scatter_dimension=0,
        tiled=True,
    )
    rows = gathered.shape[0]
    by_owner = gathered.reshape(rows, 2, replicas, shard_units).transpose(2, 0, 1, 3)
    owned = lax.all_to_all(by_owner, REP, 0, 0, tiled=True)
    terms = jnp.einsum("qtkh,qtd->qkhd", owned, all_tokens, preferred_element_type=jnp.float32)
    rounded = lax.reduce_precision(terms, exponent_bits=8, mantissa_bits=7)
    averaged = jnp.sum(rounded, axis=0) * (1.0 / replicas)
    grad_gate_weight = averaged[0:1].astype(jnp.bfloat16)
    grad_up_weight = averaged[1:2].astype(jnp.bfloat16)
    return (hidden, grad_tokens.astype(jnp.bfloat16), grad_gate_weight, grad_up_weight)


def solution(mesh):
    n_rep, n_row, n_col = (mesh.shape[a] for a in ("rep", "row", "col"))
    devices = mesh.devices.reshape(n_rep // 2, 2, n_row // 2, 2, n_col)
    fine = Mesh(devices, ("zl", "core", "x", "zh", "col"))
    in_specs = (
        P(REP, ROW),
        P("col", REP, ROW),
        P("col", REP, ROW),
        P(REP + ROW, "col"),
    )
    out_specs = (
        P(REP + ROW, "col"),
        P(REP + ("col",), ROW),
        P("col", REP, ROW),
        P("col", REP, ROW),
    )
    return jax.shard_map(body, mesh=fine, in_specs=in_specs, out_specs=out_specs, check_vma=False)
```

```python
import jax
import jax.numpy as jnp
from jax import lax
from jax.sharding import Mesh
from jax.sharding import PartitionSpec as P

REP = ("zl", "core")
ROW = ("x", "zh")


def body(tokens, gate_weight, up_weight, cotangent):
    replicas = lax.axis_size(REP)
    pair = jnp.concatenate([gate_weight, up_weight], 0)
    shard_units = pair.shape[1]
    stacked = lax.all_gather(pair, REP, axis=0, tiled=False)
    copies = jnp.broadcast_to(tokens[None], (replicas,) + tokens.shape)
    all_tokens = lax.all_to_all(copies, REP, 0, 0, tiled=True)
    hidden_units = replicas * shard_units
    partial = jnp.einsum("td,rkjd->tkrj", tokens, stacked, preferred_element_type=jnp.float32)
    partial = partial.reshape(tokens.shape[0], 2 * hidden_units)
    swap = [(0, 1), (1, 0)]
    upper = lax.axis_index("zh")
    partner_cot = lax.ppermute(cotangent, "zh", swap)
    summed = lax.psum_scatter(partial.astype(jnp.bfloat16), "x", scatter_dimension=0, tiled=True)
    summed = summed.astype(jnp.float32) + lax.ppermute(summed, "zh", swap).astype(jnp.float32)
    gate_pre = summed[:, :hidden_units]
    up_pre = summed[:, hidden_units:]
    sigmoid_val = jax.nn.sigmoid(gate_pre)
    gated = gate_pre * sigmoid_val
    hidden = (gated * up_pre).astype(jnp.bfloat16)
    pair_cot = jnp.where(
        upper == 0,
        jnp.concatenate([cotangent, partner_cot], 0),
        jnp.concatenate([partner_cot, cotangent], 0),
    )
    upstream = pair_cot.astype(jnp.float32)
    grad_gate_pre = (
        upstream * up_pre * sigmoid_val * (1.0 + gate_pre * (1.0 - sigmoid_val))
    ).astype(jnp.bfloat16)
    grad_up_pre = (upstream * gated).astype(jnp.bfloat16)
    pair_grads = jnp.concatenate([grad_gate_pre, grad_up_pre], 1)
    gathered = lax.all_gather(pair_grads, "x", axis=0, tiled=True)
    own_rows = cotangent.shape[0]
    hidden = lax.dynamic_slice_in_dim(hidden, upper * own_rows, own_rows, 0)
    grad_tokens = lax.psum_scatter(
        jnp.einsum(
            "tkrj,rkjd->td",
            gathered.reshape(gathered.shape[0], 2, replicas, shard_units),
            stacked,
            preferred_element_type=jnp.float32,
        ),
        "col",
        scatter_dimension=0,
        tiled=True,
    )
    rows = gathered.shape[0]
    by_owner = gathered.reshape(rows, 2, replicas, shard_units).transpose(2, 0, 1, 3)
    owned = lax.all_to_all(by_owner, REP, 0, 0, tiled=True)
    terms = jnp.einsum("qtkh,qtd->qkhd", owned, all_tokens, preferred_element_type=jnp.float32)
    rounded = lax.reduce_precision(terms, exponent_bits=8, mantissa_bits=7)
    averaged = jnp.sum(rounded, axis=0) * (1.0 / replicas)
    grad_gate_weight = averaged[0:1].astype(jnp.bfloat16)
    grad_up_weight = averaged[1:2].astype(jnp.bfloat16)
    return (hidden, grad_tokens.astype(jnp.bfloat16), grad_gate_weight, grad_up_weight)


def solution(mesh):
    n_rep, n_row, n_col = (mesh.shape[a] for a in ("rep", "row", "col"))
    devices = mesh.devices.reshape(n_rep // 2, 2, n_row // 2, 2, n_col)
    fine = Mesh(devices, ("zl", "core", "x", "zh", "col"))
    in_specs = (
        P(REP, ROW),
        P("col", REP, ROW),
        P("col", REP, ROW),
        P(REP + ROW, "col"),
    )
    out_specs = (
        P(REP + ROW, "col"),
        P(REP + ("col",), ROW),
        P("col", REP, ROW),
        P("col", REP, ROW),
    )
    return jax.shard_map(body, mesh=fine, in_specs=in_specs, out_specs=out_specs, check_vma=False)
```

```python
import jax
import jax.numpy as jnp
from jax import lax
from jax.sharding import Mesh
from jax.sharding import PartitionSpec as P

REP = ("zl", "core")
ROW = ("x", "zh")


def body(tokens, gate_weight, up_weight, cotangent):
    replicas = lax.axis_size(REP)
    pair = jnp.concatenate([gate_weight, up_weight], 0)
    shard_units = pair.shape[1]
    stacked = lax.all_gather(pair, REP, axis=0, tiled=False)
    copies = jnp.broadcast_to(tokens[None], (replicas,) + tokens.shape)
    all_tokens = lax.all_to_all(copies, REP, 0, 0, tiled=True)
    hidden_units = replicas * shard_units
    partial = jnp.einsum("td,rkjd->tkrj", tokens, stacked, preferred_element_type=jnp.float32)
    partial = partial.reshape(tokens.shape[0], 2 * hidden_units)
    swap = [(0, 1), (1, 0)]
    upper = lax.axis_index("zh")
    partner_cot = lax.ppermute(cotangent, "zh", swap)
    summed = lax.psum_scatter(partial, "x", scatter_dimension=0, tiled=True)
    summed = summed + lax.ppermute(summed.astype(jnp.bfloat16), "zh", swap).astype(jnp.float32)
    gate_pre = summed[:, :hidden_units]
    up_pre = summed[:, hidden_units:]
    sigmoid_val = jax.nn.sigmoid(gate_pre)
    gated = gate_pre * sigmoid_val
    hidden = (gated * up_pre).astype(jnp.bfloat16)
    pair_cot = jnp.where(
        upper == 0,
        jnp.concatenate([cotangent, partner_cot], 0),
        jnp.concatenate([partner_cot, cotangent], 0),
    )
    upstream = pair_cot.astype(jnp.float32)
    grad_gate_pre = (
        upstream * up_pre * sigmoid_val * (1.0 + gate_pre * (1.0 - sigmoid_val))
    ).astype(jnp.bfloat16)
    grad_up_pre = (upstream * gated).astype(jnp.bfloat16)
    pair_grads = jnp.concatenate([grad_gate_pre, grad_up_pre], 1)
    rows = pair_grads.shape[0]
    pieces = pair_grads.reshape(rows, 2, replicas, shard_units).transpose(2, 0, 1, 3)
    owned_part = lax.all_to_all(pieces, REP, 0, 0, tiled=True)
    n_x = lax.axis_size("x")
    both = lax.all_gather(
        jnp.stack([pair_grads.reshape(-1), owned_part.reshape(-1)]), "x", axis=1, tiled=False
    )
    gathered = both[0].reshape(n_x * rows, pair_grads.shape[1])
    owned = (
        both[1]
        .reshape(n_x, replicas, rows, 2, shard_units)
        .transpose(1, 0, 2, 3, 4)
        .reshape(replicas, n_x * rows, 2, shard_units)
    )
    own_rows = cotangent.shape[0]
    hidden = lax.dynamic_slice_in_dim(hidden, upper * own_rows, own_rows, 0)
    grad_tokens = lax.psum_scatter(
        jnp.einsum(
            "tkrj,rkjd->td",
            gathered.reshape(gathered.shape[0], 2, replicas, shard_units),
            stacked,
            preferred_element_type=jnp.float32,
        ),
        "col",
        scatter_dimension=0,
        tiled=True,
    )
    terms = jnp.einsum("qtkh,qtd->qkhd", owned, all_tokens, preferred_element_type=jnp.float32)
    rounded = lax.reduce_precision(terms, exponent_bits=8, mantissa_bits=7)
    averaged = jnp.sum(rounded, axis=0) * (1.0 / replicas)
    grad_gate_weight = averaged[0:1].astype(jnp.bfloat16)
    grad_up_weight = averaged[1:2].astype(jnp.bfloat16)
    return (hidden, grad_tokens.astype(jnp.bfloat16), grad_gate_weight, grad_up_weight)


def solution(mesh):
    n_rep, n_row, n_col = (mesh.shape[a] for a in ("rep", "row", "col"))
    devices = mesh.devices.reshape(n_rep // 2, 2, n_row // 2, 2, n_col)
    fine = Mesh(devices, ("zl", "core", "x", "zh", "col"))
    in_specs = (
        P(REP, ROW),
        P("col", REP, ROW),
        P("col", REP, ROW),
        P(REP + ROW, "col"),
    )
    out_specs = (
        P(REP + ROW, "col"),
        P(REP + ("col",), ROW),
        P("col", REP, ROW),
        P("col", REP, ROW),
    )
    return jax.shard_map(body, mesh=fine, in_specs=in_specs, out_specs=out_specs, check_vma=False)
```

```python
import jax
import jax.numpy as jnp
from jax import lax
from jax.sharding import Mesh
from jax.sharding import PartitionSpec as P

REP = ("zl", "core")
ROW = ("x", "zh")


def body(tokens, gate_weight, up_weight, cotangent):
    replicas = lax.axis_size(REP)
    pair = jnp.concatenate([gate_weight, up_weight], 0)
    shard_units = pair.shape[1]
    stacked = lax.all_gather(pair, REP, axis=0, tiled=False)
    n_col = lax.axis_size("col")
    slab = tokens.shape[0] // n_col
    mine = lax.dynamic_slice_in_dim(tokens, lax.axis_index("col") * slab, slab, 0)
    copies = jnp.broadcast_to(mine[None], (replicas,) + mine.shape)
    part = lax.all_to_all(copies, REP, 0, 0, tiled=True)
    spread = jnp.broadcast_to(part[None], (n_col,) + part.shape)
    all_tokens = lax.all_to_all(spread, "col", 0, 0, tiled=True)
    all_tokens = all_tokens.transpose(1, 0, 2, 3).reshape(replicas, n_col * slab, tokens.shape[1])
    hidden_units = replicas * shard_units
    partial = jnp.einsum("td,rkjd->tkrj", tokens, stacked, preferred_element_type=jnp.float32)
    partial = partial.reshape(tokens.shape[0], 2 * hidden_units)
    swap = [(0, 1), (1, 0)]
    upper = lax.axis_index("zh")
    partner_cot = lax.ppermute(cotangent, "zh", swap)
    summed = lax.psum_scatter(partial, "x", scatter_dimension=0, tiled=True)
    summed = summed + lax.ppermute(summed.astype(jnp.bfloat16), "zh", swap).astype(jnp.float32)
    gate_pre = summed[:, :hidden_units]
    up_pre = summed[:, hidden_units:]
    sigmoid_val = jax.nn.sigmoid(gate_pre)
    gated = gate_pre * sigmoid_val
    hidden = (gated * up_pre).astype(jnp.bfloat16)
    pair_cot = jnp.where(
        upper == 0,
        jnp.concatenate([cotangent, partner_cot], 0),
        jnp.concatenate([partner_cot, cotangent], 0),
    )
    upstream = pair_cot.astype(jnp.float32)
    grad_gate_pre = (
        upstream * up_pre * sigmoid_val * (1.0 + gate_pre * (1.0 - sigmoid_val))
    ).astype(jnp.bfloat16)
    grad_up_pre = (upstream * gated).astype(jnp.bfloat16)
    pair_grads = jnp.concatenate([grad_gate_pre, grad_up_pre], 1)
    gathered = lax.all_gather(pair_grads, "x", axis=0, tiled=True)
    own_rows = cotangent.shape[0]
    hidden = lax.dynamic_slice_in_dim(hidden, upper * own_rows, own_rows, 0)
    grad_tokens = lax.psum_scatter(
        jnp.einsum(
            "tkrj,rkjd->td",
            gathered.reshape(gathered.shape[0], 2, replicas, shard_units),
            stacked,
            preferred_element_type=jnp.float32,
        ),
        "col",
        scatter_dimension=0,
        tiled=True,
    )
    rows = gathered.shape[0]
    by_owner = gathered.reshape(rows, 2, replicas, shard_units).transpose(2, 0, 1, 3)
    owned = lax.all_to_all(by_owner, REP, 0, 0, tiled=True)
    terms = jnp.einsum("qtkh,qtd->qkhd", owned, all_tokens, preferred_element_type=jnp.float32)
    rounded = lax.reduce_precision(terms, exponent_bits=8, mantissa_bits=7)
    averaged = jnp.sum(rounded, axis=0) * (1.0 / replicas)
    grad_gate_weight = averaged[0:1].astype(jnp.bfloat16)
    grad_up_weight = averaged[1:2].astype(jnp.bfloat16)
    return (hidden, grad_tokens.astype(jnp.bfloat16), grad_gate_weight, grad_up_weight)


def solution(mesh):
    n_rep, n_row, n_col = (mesh.shape[a] for a in ("rep", "row", "col"))
    devices = mesh.devices.reshape(n_rep // 2, 2, n_row // 2, 2, n_col)
    fine = Mesh(devices, ("zl", "core", "x", "zh", "col"))
    in_specs = (
        P(REP, ROW),
        P("col", REP, ROW),
        P("col", REP, ROW),
        P(REP + ROW, "col"),
    )
    out_specs = (
        P(REP + ROW, "col"),
        P(REP + ("col",), ROW),
        P("col", REP, ROW),
        P("col", REP, ROW),
    )
    return jax.shard_map(body, mesh=fine, in_specs=in_specs, out_specs=out_specs, check_vma=False)
```

```python
import jax
import jax.numpy as jnp
from jax import lax
from jax.sharding import Mesh
from jax.sharding import PartitionSpec as P

REP = ("zl", "core")
ROW = ("x", "zh")


def body(tokens, gate_weight, up_weight, cotangent):
    replicas = lax.axis_size(REP)
    pair = jnp.concatenate([gate_weight, up_weight], 0)
    shard_units = pair.shape[1]
    stacked = lax.all_gather(pair, REP, axis=0, tiled=False)
    n_col = lax.axis_size("col")
    slab = tokens.shape[0] // n_col
    mine = lax.dynamic_slice_in_dim(tokens, lax.axis_index("col") * slab, slab, 0)
    copies = jnp.broadcast_to(mine[None], (replicas,) + mine.shape)
    part = lax.all_to_all(copies, REP, 0, 0, tiled=True)
    spread = jnp.broadcast_to(part[None], (n_col,) + part.shape)
    all_tokens = lax.all_to_all(spread, "col", 0, 0, tiled=True)
    all_tokens = all_tokens.transpose(1, 0, 2, 3).reshape(replicas, n_col * slab, tokens.shape[1])
    hidden_units = replicas * shard_units
    partial = jnp.einsum("td,rkjd->tkrj", tokens, stacked, preferred_element_type=jnp.float32)
    partial = partial.reshape(tokens.shape[0], 2 * hidden_units)
    swap = [(0, 1), (1, 0)]
    upper = lax.axis_index("zh")
    partner_cot = lax.ppermute(cotangent, "zh", swap)
    summed = lax.psum_scatter(partial.astype(jnp.bfloat16), "x", scatter_dimension=0, tiled=True)
    summed = summed.astype(jnp.float32) + lax.ppermute(summed, "zh", swap).astype(jnp.float32)
    gate_pre = summed[:, :hidden_units]
    up_pre = summed[:, hidden_units:]
    sigmoid_val = jax.nn.sigmoid(gate_pre)
    gated = gate_pre * sigmoid_val
    hidden = (gated * up_pre).astype(jnp.bfloat16)
    pair_cot = jnp.where(
        upper == 0,
        jnp.concatenate([cotangent, partner_cot], 0),
        jnp.concatenate([partner_cot, cotangent], 0),
    )
    upstream = pair_cot.astype(jnp.float32)
    grad_gate_pre = (
        upstream * up_pre * sigmoid_val * (1.0 + gate_pre * (1.0 - sigmoid_val))
    ).astype(jnp.bfloat16)
    grad_up_pre = (upstream * gated).astype(jnp.bfloat16)
    pair_grads = jnp.concatenate([grad_gate_pre, grad_up_pre], 1)
    gathered = lax.all_gather(pair_grads, "x", axis=0, tiled=True)
    own_rows = cotangent.shape[0]
    hidden = lax.dynamic_slice_in_dim(hidden, upper * own_rows, own_rows, 0)
    grad_tokens = lax.psum_scatter(
        jnp.einsum(
            "tkrj,rkjd->td",
            gathered.reshape(gathered.shape[0], 2, replicas, shard_units),
            stacked,
            preferred_element_type=jnp.float32,
        ),
        "col",
        scatter_dimension=0,
        tiled=True,
    )
    rows = gathered.shape[0]
    by_owner = gathered.reshape(rows, 2, replicas, shard_units).transpose(2, 0, 1, 3)
    owned = lax.all_to_all(by_owner, REP, 0, 0, tiled=True)
    terms = jnp.einsum("qtkh,qtd->qkhd", owned, all_tokens, preferred_element_type=jnp.float32)
    rounded = lax.reduce_precision(terms, exponent_bits=8, mantissa_bits=7)
    averaged = jnp.sum(rounded, axis=0) * (1.0 / replicas)
    grad_gate_weight = averaged[0:1].astype(jnp.bfloat16)
    grad_up_weight = averaged[1:2].astype(jnp.bfloat16)
    return (hidden, grad_tokens.astype(jnp.bfloat16), grad_gate_weight, grad_up_weight)


def solution(mesh):
    n_rep, n_row, n_col = (mesh.shape[a] for a in ("rep", "row", "col"))
    devices = mesh.devices.reshape(n_rep // 2, 2, n_row // 2, 2, n_col)
    fine = Mesh(devices, ("zl", "core", "x", "zh", "col"))
    in_specs = (
        P(REP, ROW),
        P("col", REP, ROW),
        P("col", REP, ROW),
        P(REP + ROW, "col"),
    )
    out_specs = (
        P(REP + ROW, "col"),
        P(REP + ("col",), ROW),
        P("col", REP, ROW),
        P("col", REP, ROW),
    )
    return jax.shard_map(body, mesh=fine, in_specs=in_specs, out_specs=out_specs, check_vma=False)
```

```python
import jax
import jax.numpy as jnp
from jax import lax
from jax.sharding import Mesh
from jax.sharding import PartitionSpec as P

REP = ("zl", "core")
ROW = ("x", "zh")


def body(tokens, gate_weight, up_weight, cotangent):
    replicas = lax.axis_size(REP)
    pair = jnp.concatenate([gate_weight, up_weight], 0)
    shard_units = pair.shape[1]
    stacked = lax.all_gather(pair, REP, axis=0, tiled=False)
    n_col = lax.axis_size("col")
    slab = tokens.shape[0] // n_col
    mine = lax.dynamic_slice_in_dim(tokens, lax.axis_index("col") * slab, slab, 0)
    copies = jnp.broadcast_to(mine[None], (replicas,) + mine.shape)
    part = lax.all_to_all(copies, REP, 0, 0, tiled=True)
    spread = jnp.broadcast_to(part[None], (n_col,) + part.shape)
    all_tokens = lax.all_to_all(spread, "col", 0, 0, tiled=True)
    all_tokens = all_tokens.transpose(1, 0, 2, 3).reshape(replicas, n_col * slab, tokens.shape[1])
    hidden_units = replicas * shard_units
    partial = jnp.einsum("td,rkjd->tkrj", tokens, stacked, preferred_element_type=jnp.float32)
    partial = partial.reshape(tokens.shape[0], 2 * hidden_units)
    swap = [(0, 1), (1, 0)]
    upper = lax.axis_index("zh")
    partner_cot = lax.ppermute(cotangent, "zh", swap)
    summed = lax.psum_scatter(partial.astype(jnp.bfloat16), "x", scatter_dimension=0, tiled=True)
    summed = summed.astype(jnp.float32) + lax.ppermute(summed, "zh", swap).astype(jnp.float32)
    gate_pre = summed[:, :hidden_units]
    up_pre = summed[:, hidden_units:]
    sigmoid_val = jax.nn.sigmoid(gate_pre)
    gated = gate_pre * sigmoid_val
    hidden = (gated * up_pre).astype(jnp.bfloat16)
    pair_cot = jnp.where(
        upper == 0,
        jnp.concatenate([cotangent, partner_cot], 0),
        jnp.concatenate([partner_cot, cotangent], 0),
    )
    upstream = pair_cot.astype(jnp.float32)
    grad_gate_pre = (
        upstream * up_pre * sigmoid_val * (1.0 + gate_pre * (1.0 - sigmoid_val))
    ).astype(jnp.bfloat16)
    grad_up_pre = (upstream * gated).astype(jnp.bfloat16)
    pair_grads = jnp.concatenate([grad_gate_pre, grad_up_pre], 1)
    gathered = lax.all_gather(pair_grads, "x", axis=0, tiled=True)
    own_rows = cotangent.shape[0]
    hidden = lax.dynamic_slice_in_dim(hidden, upper * own_rows, own_rows, 0)
    grad_tokens = lax.psum_scatter(
        jnp.einsum(
            "tkrj,rkjd->td",
            gathered.reshape(gathered.shape[0], 2, replicas, shard_units),
            stacked,
            preferred_element_type=jnp.float32,
        ).astype(jnp.bfloat16),
        "col",
        scatter_dimension=0,
        tiled=True,
    )
    rows = gathered.shape[0]
    by_owner = gathered.reshape(rows, 2, replicas, shard_units).transpose(2, 0, 1, 3)
    owned = lax.all_to_all(by_owner, REP, 0, 0, tiled=True)
    terms = jnp.einsum("qtkh,qtd->qkhd", owned, all_tokens, preferred_element_type=jnp.float32)
    rounded = lax.reduce_precision(terms, exponent_bits=8, mantissa_bits=7)
    averaged = jnp.sum(rounded, axis=0) * (1.0 / replicas)
    grad_gate_weight = averaged[0:1].astype(jnp.bfloat16)
    grad_up_weight = averaged[1:2].astype(jnp.bfloat16)
    return (hidden, grad_tokens.astype(jnp.bfloat16), grad_gate_weight, grad_up_weight)


def solution(mesh):
    n_rep, n_row, n_col = (mesh.shape[a] for a in ("rep", "row", "col"))
    devices = mesh.devices.reshape(n_rep // 2, 2, n_row // 2, 2, n_col)
    fine = Mesh(devices, ("zl", "core", "x", "zh", "col"))
    in_specs = (
        P(REP, ROW),
        P("col", REP, ROW),
        P("col", REP, ROW),
        P(REP + ROW, "col"),
    )
    out_specs = (
        P(REP + ROW, "col"),
        P(REP + ("col",), ROW),
        P("col", REP, ROW),
        P("col", REP, ROW),
    )
    return jax.shard_map(body, mesh=fine, in_specs=in_specs, out_specs=out_specs, check_vma=False)
```

```python
import jax
import jax.numpy as jnp
from jax import lax
from jax.sharding import Mesh
from jax.sharding import PartitionSpec as P

REP = ("zl", "core")
ROW = ("x", "zh")


def body(tokens, gate_weight, up_weight, cotangent):
    replicas = lax.axis_size(REP)
    pair = jnp.concatenate([gate_weight, up_weight], 0)
    shard_units = pair.shape[1]
    stacked = lax.all_gather(pair, REP, axis=0, tiled=False)
    n_col = lax.axis_size("col")
    slab = tokens.shape[0] // n_col
    mine = lax.dynamic_slice_in_dim(tokens, lax.axis_index("col") * slab, slab, 0)
    copies = jnp.broadcast_to(mine[None], (replicas,) + mine.shape)
    part = lax.all_to_all(copies, REP, 0, 0, tiled=True)
    spread = jnp.broadcast_to(part[None], (n_col,) + part.shape)
    all_tokens = lax.all_to_all(spread, "col", 0, 0, tiled=True)
    all_tokens = all_tokens.transpose(1, 0, 2, 3).reshape(replicas, n_col * slab, tokens.shape[1])
    hidden_units = replicas * shard_units
    swap = [(0, 1), (1, 0)]
    partner_cot = lax.ppermute(cotangent, "zh", swap)
    tokens, partner_cot = lax.optimization_barrier((tokens, partner_cot))
    partial = jnp.einsum("td,rkjd->tkrj", tokens, stacked, preferred_element_type=jnp.float32)
    partial = partial.reshape(tokens.shape[0], 2 * hidden_units)
    swap = [(0, 1), (1, 0)]
    upper = lax.axis_index("zh")
    summed = lax.psum_scatter(partial.astype(jnp.bfloat16), "x", scatter_dimension=0, tiled=True)
    summed = summed.astype(jnp.float32) + lax.ppermute(summed, "zh", swap).astype(jnp.float32)
    gate_pre = summed[:, :hidden_units]
    up_pre = summed[:, hidden_units:]
    sigmoid_val = jax.nn.sigmoid(gate_pre)
    gated = gate_pre * sigmoid_val
    hidden = (gated * up_pre).astype(jnp.bfloat16)
    pair_cot = jnp.where(
        upper == 0,
        jnp.concatenate([cotangent, partner_cot], 0),
        jnp.concatenate([partner_cot, cotangent], 0),
    )
    upstream = pair_cot.astype(jnp.float32)
    grad_gate_pre = (
        upstream * up_pre * sigmoid_val * (1.0 + gate_pre * (1.0 - sigmoid_val))
    ).astype(jnp.bfloat16)
    grad_up_pre = (upstream * gated).astype(jnp.bfloat16)
    pair_grads = jnp.concatenate([grad_gate_pre, grad_up_pre], 1)
    gathered = lax.all_gather(pair_grads, "x", axis=0, tiled=True)
    own_rows = cotangent.shape[0]
    hidden = lax.dynamic_slice_in_dim(hidden, upper * own_rows, own_rows, 0)
    grad_tokens = lax.psum_scatter(
        jnp.einsum(
            "tkrj,rkjd->td",
            gathered.reshape(gathered.shape[0], 2, replicas, shard_units),
            stacked,
            preferred_element_type=jnp.float32,
        ).astype(jnp.bfloat16),
        "col",
        scatter_dimension=0,
        tiled=True,
    )
    rows = gathered.shape[0]
    by_owner = gathered.reshape(rows, 2, replicas, shard_units).transpose(2, 0, 1, 3)
    owned = lax.all_to_all(by_owner, REP, 0, 0, tiled=True)
    terms = jnp.einsum("qtkh,qtd->qkhd", owned, all_tokens, preferred_element_type=jnp.float32)
    rounded = lax.reduce_precision(terms, exponent_bits=8, mantissa_bits=7)
    averaged = jnp.sum(rounded, axis=0) * (1.0 / replicas)
    grad_gate_weight = averaged[0:1].astype(jnp.bfloat16)
    grad_up_weight = averaged[1:2].astype(jnp.bfloat16)
    return (hidden, grad_tokens.astype(jnp.bfloat16), grad_gate_weight, grad_up_weight)


def solution(mesh):
    n_rep, n_row, n_col = (mesh.shape[a] for a in ("rep", "row", "col"))
    devices = mesh.devices.reshape(n_rep // 2, 2, n_row // 2, 2, n_col)
    fine = Mesh(devices, ("zl", "core", "x", "zh", "col"))
    in_specs = (
        P(REP, ROW),
        P("col", REP, ROW),
        P("col", REP, ROW),
        P(REP + ROW, "col"),
    )
    out_specs = (
        P(REP + ROW, "col"),
        P(REP + ("col",), ROW),
        P("col", REP, ROW),
        P("col", REP, ROW),
    )
    return jax.shard_map(body, mesh=fine, in_specs=in_specs, out_specs=out_specs, check_vma=False)
```

```python
import jax
import jax.numpy as jnp
from jax import lax
from jax.sharding import Mesh
from jax.sharding import PartitionSpec as P

REP = ("zl", "core")
ROW = ("x", "zh")


def body(tokens, gate_weight, up_weight, cotangent):
    replicas = lax.axis_size(REP)
    pair = jnp.concatenate([gate_weight, up_weight], 0)
    shard_units = pair.shape[1]
    stacked = lax.all_gather(pair, REP, axis=0, tiled=False)
    n_col = lax.axis_size("col")
    slab = tokens.shape[0] // n_col
    mine = lax.dynamic_slice_in_dim(tokens, lax.axis_index("col") * slab, slab, 0)
    copies = jnp.broadcast_to(mine[None], (replicas,) + mine.shape)
    part = lax.all_to_all(copies, REP, 0, 0, tiled=True)
    spread = jnp.broadcast_to(part[None], (n_col,) + part.shape)
    all_tokens = lax.all_to_all(spread, "col", 0, 0, tiled=True)
    all_tokens = all_tokens.transpose(1, 0, 2, 3).reshape(replicas, n_col * slab, tokens.shape[1])
    hidden_units = replicas * shard_units
    swap = [(0, 1), (1, 0)]
    partner_cot = lax.ppermute(cotangent, "zh", swap)
    tokens, partner_cot, all_tokens = lax.optimization_barrier((tokens, partner_cot, all_tokens))
    partial = jnp.einsum("td,rkjd->tkrj", tokens, stacked, preferred_element_type=jnp.float32)
    partial = partial.reshape(tokens.shape[0], 2 * hidden_units)
    swap = [(0, 1), (1, 0)]
    upper = lax.axis_index("zh")
    summed = lax.psum_scatter(partial.astype(jnp.bfloat16), "x", scatter_dimension=0, tiled=True)
    summed = summed.astype(jnp.float32) + lax.ppermute(summed, "zh", swap).astype(jnp.float32)
    gate_pre = summed[:, :hidden_units]
    up_pre = summed[:, hidden_units:]
    sigmoid_val = jax.nn.sigmoid(gate_pre)
    gated = gate_pre * sigmoid_val
    hidden = (gated * up_pre).astype(jnp.bfloat16)
    pair_cot = jnp.where(
        upper == 0,
        jnp.concatenate([cotangent, partner_cot], 0),
        jnp.concatenate([partner_cot, cotangent], 0),
    )
    upstream = pair_cot.astype(jnp.float32)
    grad_gate_pre = (
        upstream * up_pre * sigmoid_val * (1.0 + gate_pre * (1.0 - sigmoid_val))
    ).astype(jnp.bfloat16)
    grad_up_pre = (upstream * gated).astype(jnp.bfloat16)
    pair_grads = jnp.concatenate([grad_gate_pre, grad_up_pre], 1)
    gathered = lax.all_gather(pair_grads, "x", axis=0, tiled=True)
    own_rows = cotangent.shape[0]
    hidden = lax.dynamic_slice_in_dim(hidden, upper * own_rows, own_rows, 0)
    grad_tokens = lax.psum_scatter(
        jnp.einsum(
            "tkrj,rkjd->td",
            gathered.reshape(gathered.shape[0], 2, replicas, shard_units),
            stacked,
            preferred_element_type=jnp.float32,
        ).astype(jnp.bfloat16),
        "col",
        scatter_dimension=0,
        tiled=True,
    )
    rows = gathered.shape[0]
    by_owner = gathered.reshape(rows, 2, replicas, shard_units).transpose(2, 0, 1, 3)
    owned = lax.all_to_all(by_owner, REP, 0, 0, tiled=True)
    terms = jnp.einsum("qtkh,qtd->qkhd", owned, all_tokens, preferred_element_type=jnp.float32)
    rounded = lax.reduce_precision(terms, exponent_bits=8, mantissa_bits=7)
    averaged = jnp.sum(rounded, axis=0) * (1.0 / replicas)
    grad_gate_weight = averaged[0:1].astype(jnp.bfloat16)
    grad_up_weight = averaged[1:2].astype(jnp.bfloat16)
    return (hidden, grad_tokens.astype(jnp.bfloat16), grad_gate_weight, grad_up_weight)


def solution(mesh):
    n_rep, n_row, n_col = (mesh.shape[a] for a in ("rep", "row", "col"))
    devices = mesh.devices.reshape(n_rep // 2, 2, n_row // 2, 2, n_col)
    fine = Mesh(devices, ("zl", "core", "x", "zh", "col"))
    in_specs = (
        P(REP, ROW),
        P("col", REP, ROW),
        P("col", REP, ROW),
        P(REP + ROW, "col"),
    )
    out_specs = (
        P(REP + ROW, "col"),
        P(REP + ("col",), ROW),
        P("col", REP, ROW),
        P("col", REP, ROW),
    )
    return jax.shard_map(body, mesh=fine, in_specs=in_specs, out_specs=out_specs, check_vma=False)
```

```python
import jax
import jax.numpy as jnp
from jax import lax
from jax.sharding import Mesh
from jax.sharding import PartitionSpec as P

REP = ("zl", "core")
ROW = ("x", "zh")


def body(tokens, gate_weight, up_weight, cotangent):
    replicas = lax.axis_size(REP)
    pair = jnp.concatenate([gate_weight, up_weight], 0)
    shard_units = pair.shape[1]
    stacked = lax.all_gather(pair, REP, axis=0, tiled=False)
    n_col = lax.axis_size("col")
    slab = tokens.shape[0] // n_col
    mine = lax.dynamic_slice_in_dim(tokens, lax.axis_index("col") * slab, slab, 0)
    copies = jnp.broadcast_to(mine[None], (replicas,) + mine.shape)
    part = lax.all_to_all(copies, REP, 0, 0, tiled=True)
    spread = jnp.broadcast_to(part[None], (n_col,) + part.shape)
    all_tokens = lax.all_to_all(spread, "col", 0, 0, tiled=True)
    all_tokens = all_tokens.transpose(1, 0, 2, 3).reshape(replicas, n_col * slab, tokens.shape[1])
    hidden_units = replicas * shard_units
    swap = [(0, 1), (1, 0)]
    partner_cot = lax.ppermute(cotangent, "zh", swap)
    tokens, partner_cot = lax.optimization_barrier((tokens, partner_cot))
    partial = jnp.einsum("td,rkjd->tkrj", tokens, stacked, preferred_element_type=jnp.float32)
    partial = partial.reshape(tokens.shape[0], 2 * hidden_units)
    swap = [(0, 1), (1, 0)]
    upper = lax.axis_index("zh")
    summed = lax.psum_scatter(partial.astype(jnp.bfloat16), "x", scatter_dimension=0, tiled=True)
    summed = summed.astype(jnp.float32) + lax.ppermute(summed, "zh", swap).astype(jnp.float32)
    gate_pre = summed[:, :hidden_units]
    up_pre = summed[:, hidden_units:]
    sigmoid_val = jax.nn.sigmoid(gate_pre)
    gated = gate_pre * sigmoid_val
    hidden = (gated * up_pre).astype(jnp.bfloat16)
    pair_cot = jnp.where(
        upper == 0,
        jnp.concatenate([cotangent, partner_cot], 0),
        jnp.concatenate([partner_cot, cotangent], 0),
    )
    upstream = pair_cot.astype(jnp.float32)
    grad_gate_pre = (
        upstream * up_pre * sigmoid_val * (1.0 + gate_pre * (1.0 - sigmoid_val))
    ).astype(jnp.bfloat16)
    grad_up_pre = (upstream * gated).astype(jnp.bfloat16)
    pair_grads = jnp.concatenate([grad_gate_pre, grad_up_pre], 1)
    rows = pair_grads.shape[0]
    pieces = pair_grads.reshape(rows, 2, replicas, shard_units).transpose(2, 0, 1, 3)
    owned_part = lax.all_to_all(pieces, REP, 0, 0, tiled=True)
    gathered = lax.all_gather(pair_grads, "x", axis=0, tiled=True)
    owned = lax.all_gather(owned_part, "x", axis=1, tiled=True)
    own_rows = cotangent.shape[0]
    hidden = lax.dynamic_slice_in_dim(hidden, upper * own_rows, own_rows, 0)
    grad_tokens = lax.psum_scatter(
        jnp.einsum(
            "tkrj,rkjd->td",
            gathered.reshape(gathered.shape[0], 2, replicas, shard_units),
            stacked,
            preferred_element_type=jnp.float32,
        ).astype(jnp.bfloat16),
        "col",
        scatter_dimension=0,
        tiled=True,
    )
    terms = jnp.einsum("qtkh,qtd->qkhd", owned, all_tokens, preferred_element_type=jnp.float32)
    rounded = lax.reduce_precision(terms, exponent_bits=8, mantissa_bits=7)
    averaged = jnp.sum(rounded, axis=0) * (1.0 / replicas)
    grad_gate_weight = averaged[0:1].astype(jnp.bfloat16)
    grad_up_weight = averaged[1:2].astype(jnp.bfloat16)
    return (hidden, grad_tokens.astype(jnp.bfloat16), grad_gate_weight, grad_up_weight)


def solution(mesh):
    n_rep, n_row, n_col = (mesh.shape[a] for a in ("rep", "row", "col"))
    devices = mesh.devices.reshape(n_rep // 2, 2, n_row // 2, 2, n_col)
    fine = Mesh(devices, ("zl", "core", "x", "zh", "col"))
    in_specs = (
        P(REP, ROW),
        P("col", REP, ROW),
        P("col", REP, ROW),
        P(REP + ROW, "col"),
    )
    out_specs = (
        P(REP + ROW, "col"),
        P(REP + ("col",), ROW),
        P("col", REP, ROW),
        P("col", REP, ROW),
    )
    return jax.shard_map(body, mesh=fine, in_specs=in_specs, out_specs=out_specs, check_vma=False)
```

```python
import jax
import jax.numpy as jnp
from jax import lax
from jax.sharding import Mesh
from jax.sharding import PartitionSpec as P

REP = ("zl", "core")
ROW = ("x", "zh")


def body(tokens, gate_weight, up_weight, cotangent):
    replicas = lax.axis_size(REP)
    pair = jnp.concatenate([gate_weight, up_weight], 0)
    shard_units = pair.shape[1]
    stacked = lax.all_gather(pair, REP, axis=0, tiled=False)
    n_col = lax.axis_size("col")
    slab = tokens.shape[0] // n_col
    mine = lax.dynamic_slice_in_dim(tokens, lax.axis_index("col") * slab, slab, 0)
    copies = jnp.broadcast_to(mine[None], (replicas,) + mine.shape)
    part = lax.all_to_all(copies, REP, 0, 0, tiled=True)
    tokens, part = lax.optimization_barrier((tokens, part))
    spread = jnp.broadcast_to(part[None], (n_col,) + part.shape)
    all_tokens = lax.all_to_all(spread, "col", 0, 0, tiled=True)
    all_tokens = all_tokens.transpose(1, 0, 2, 3).reshape(replicas, n_col * slab, tokens.shape[1])
    hidden_units = replicas * shard_units
    swap = [(0, 1), (1, 0)]
    partner_cot = lax.ppermute(cotangent, "zh", swap)
    tokens, partner_cot = lax.optimization_barrier((tokens, partner_cot))
    partial = jnp.einsum("td,rkjd->tkrj", tokens, stacked, preferred_element_type=jnp.float32)
    partial = partial.reshape(tokens.shape[0], 2 * hidden_units)
    swap = [(0, 1), (1, 0)]
    upper = lax.axis_index("zh")
    summed = lax.psum_scatter(partial.astype(jnp.bfloat16), "x", scatter_dimension=0, tiled=True)
    summed = summed.astype(jnp.float32) + lax.ppermute(summed, "zh", swap).astype(jnp.float32)
    gate_pre = summed[:, :hidden_units]
    up_pre = summed[:, hidden_units:]
    sigmoid_val = jax.nn.sigmoid(gate_pre)
    gated = gate_pre * sigmoid_val
    hidden = (gated * up_pre).astype(jnp.bfloat16)
    pair_cot = jnp.where(
        upper == 0,
        jnp.concatenate([cotangent, partner_cot], 0),
        jnp.concatenate([partner_cot, cotangent], 0),
    )
    upstream = pair_cot.astype(jnp.float32)
    grad_gate_pre = (
        upstream * up_pre * sigmoid_val * (1.0 + gate_pre * (1.0 - sigmoid_val))
    ).astype(jnp.bfloat16)
    grad_up_pre = (upstream * gated).astype(jnp.bfloat16)
    pair_grads = jnp.concatenate([grad_gate_pre, grad_up_pre], 1)
    gathered = lax.all_gather(pair_grads, "x", axis=0, tiled=True)
    own_rows = cotangent.shape[0]
    hidden = lax.dynamic_slice_in_dim(hidden, upper * own_rows, own_rows, 0)
    grad_tokens = lax.psum_scatter(
        jnp.einsum(
            "tkrj,rkjd->td",
            gathered.reshape(gathered.shape[0], 2, replicas, shard_units),
            stacked,
            preferred_element_type=jnp.float32,
        ).astype(jnp.bfloat16),
        "col",
        scatter_dimension=0,
        tiled=True,
    )
    rows = gathered.shape[0]
    by_owner = gathered.reshape(rows, 2, replicas, shard_units).transpose(2, 0, 1, 3)
    owned = lax.all_to_all(by_owner, REP, 0, 0, tiled=True)
    terms = jnp.einsum("qtkh,qtd->qkhd", owned, all_tokens, preferred_element_type=jnp.float32)
    rounded = lax.reduce_precision(terms, exponent_bits=8, mantissa_bits=7)
    averaged = jnp.sum(rounded, axis=0) * (1.0 / replicas)
    grad_gate_weight = averaged[0:1].astype(jnp.bfloat16)
    grad_up_weight = averaged[1:2].astype(jnp.bfloat16)
    return (hidden, grad_tokens.astype(jnp.bfloat16), grad_gate_weight, grad_up_weight)


def solution(mesh):
    n_rep, n_row, n_col = (mesh.shape[a] for a in ("rep", "row", "col"))
    devices = mesh.devices.reshape(n_rep // 2, 2, n_row // 2, 2, n_col)
    fine = Mesh(devices, ("zl", "core", "x", "zh", "col"))
    in_specs = (
        P(REP, ROW),
        P("col", REP, ROW),
        P("col", REP, ROW),
        P(REP + ROW, "col"),
    )
    out_specs = (
        P(REP + ROW, "col"),
        P(REP + ("col",), ROW),
        P("col", REP, ROW),
        P("col", REP, ROW),
    )
    return jax.shard_map(body, mesh=fine, in_specs=in_specs, out_specs=out_specs, check_vma=False)
```
